768 devices in a mesh: fsdp: 192 (over y, z, core), ctx: 4 (over x).
Axes of the slice: x: 4, y: 8, z: 12, core: 2. Of those that a mesh axis runs over, the one named last changes fastest.
Arguments:
- queries: bfloat16 [79872, 3072], P(('fsdp', 'ctx')), may hold values from -6 to 6
- keys: bfloat16 [79872, 3072], P(('fsdp', 'ctx')), may hold values from -6 to 6
- values: bfloat16 [79872, 3072], P(('fsdp', 'ctx')), may hold values from -6 to 6
- norm_gain: float32 [3072], replicated, may hold values from 0.1 to 1.9
- out_weight: bfloat16 [3072, 3072], P('fsdp', 'ctx'), may hold values from -0.109375 to 0.109375
Outputs:
- layer_out: bfloat16 [79872, 3072], P('fsdp', 'ctx')
The draws below stay inside these ranges and needn't reach their ends.
All inputs are finite; a program needn't handle non-finite values.
Results may differ from the reference program's by a relative error of at most 0.0061.
Values may be sent and summed in bfloat16 or wider, within the bound.
No kernel may reach another device: no remote copies, remote signals or barrier semaphores. Data moves between devices by JAX's collectives and lax.ppermute only.
A program may use at most 32 MiB of HBM per device.

```python
import jax
import jax.numpy as jnp
from jax import lax

HEADS = 32
HEAD_DIM = 96
D = 3072
TOK_DEV = 104
HD = 3072
SEQ_LEN = 416
TOKENS = 79872
N_CTX = 4


def steps_of(key, extent, pieces, least, largest):
    factor_of, own = 1.0, jax.random.fold_in(key, 6)
    for dim, blocks in pieces:
        steps = jnp.exp(jax.random.uniform(jax.random.fold_in(own, dim), (blocks,), jnp.float32, least / len(pieces), largest / len(pieces)))
        factor_of = factor_of * jnp.repeat(steps, extent[dim] // blocks).reshape([-1 if axis == dim else 1 for axis in range(len(extent))])
    return factor_of


def gaussian(stream_key, dims, scale, reach, shards=(), dtype=jnp.bfloat16):
    factor_of = steps_of(stream_key, dims, shards, -0.22, 0.18) if shards else 1.0
    values = jax.random.normal(stream_key, dims, jnp.float32) * scale * factor_of
    return jnp.minimum(jnp.maximum(values, -reach), reach).astype(dtype)


def setup_inputs(seed: int = 0) -> dict:
    streams_of = jax.random.split(jax.random.key(seed), 6)
    return {
        "queries": gaussian(streams_of[0], (TOKENS, HD), 1.0, 6.0, ((0, 768),)),
        "keys": gaussian(streams_of[1], (TOKENS, HD), 1.0, 6.0, ((0, 768),)),
        "values": gaussian(streams_of[2], (TOKENS, HD), 1.0, 6.0, ((0, 768),)),
        "norm_gain": jnp.clip(1.0 + 0.18 * jax.random.normal(streams_of[3], (HD,), jnp.float32), 0.1, 1.9),
        "out_weight": gaussian(streams_of[4], (HD, D), HD ** -0.5, 0.109375, ((0, 192), (1, 4))),
    }


def one_sequence(items, norm_gain):
    q_blocks, k_blocks, v_blocks = items
    causal = jnp.arange(TOK_DEV)[:, None] >= jnp.arange(TOK_DEV)[None, :]

    def step(running, parts):
        q_block = parts[0].astype(jnp.float32)
        k_block = parts[1].astype(jnp.float32)
        v_block = parts[2].astype(jnp.float32)
        scores = jnp.einsum('thd,shd->hts', q_block, k_block)
        scores = jnp.where(causal, scores, 0.0).astype(jnp.bfloat16)
        intra = jnp.einsum('hts,shd->thd', scores.astype(jnp.float32), v_block)
        local_state = jnp.einsum('shd,she->hde', k_block, v_block).astype(jnp.bfloat16)
        prefix_state = running.astype(jnp.bfloat16)
        inter = jnp.einsum('thd,hde->the', q_block, prefix_state.astype(jnp.float32))
        attn = (intra + inter).reshape(TOK_DEV, HD)
        mean_sq = lax.optimization_barrier(jnp.mean(attn * attn, axis=-1, keepdims=True))
        normed = (attn * lax.rsqrt(mean_sq + 1e-05) * norm_gain).astype(jnp.bfloat16)
        return (running + local_state.astype(jnp.float32), normed)
    start = jnp.zeros((HEADS, HEAD_DIM, HEAD_DIM), jnp.float32)
    final_state, normed_seq = lax.scan(step, start, (q_blocks, k_blocks, v_blocks))
    return normed_seq

def reference(queries, keys, values, norm_gain, out_weight):
    sequences = TOKENS // SEQ_LEN
    shape = (sequences, N_CTX, TOK_DEV, HEADS, HEAD_DIM)
    normed_all = lax.map(lambda items: one_sequence(items, norm_gain), (queries.reshape(shape), keys.reshape(shape), values.reshape(shape)))
    normed_all = normed_all.reshape(TOKENS, HD)
    return jnp.dot(normed_all, out_weight, preferred_element_type=jnp.float32).astype(jnp.bfloat16)
```

```python
import jax
import jax.numpy as jnp
import numpy as np
from jax import lax
from jax.sharding import Mesh
from jax.sharding import PartitionSpec as P

HEADS = 32
HEAD_DIM = 96


def make_on_device(n_ctx, n_core):
    def on_device(queries, keys, values, norm_gain, out_weight):
        w_half = lax.all_gather(out_weight, "chips", axis=0, tiled=True)
        w_both = lax.all_gather(w_half, "core", axis=0, tiled=False)
        rows, cols = out_weight.shape
        weight_block = (
            w_both.reshape(n_core, -1, rows, cols).transpose(1, 0, 2, 3).reshape(-1, cols)
        )

        tok_rows = queries.shape[0]
        q_heads = queries.reshape(tok_rows, HEADS, HEAD_DIM)
        k_heads = keys.reshape(tok_rows, HEADS, HEAD_DIM)
        v_heads = values.reshape(tok_rows, HEADS, HEAD_DIM)
        local_state = jnp.einsum("shd,she->hde", k_heads, v_heads, preferred_element_type=jnp.float32)
        state_bf = local_state.astype(jnp.bfloat16)
        prefix_f32 = jnp.zeros(local_state.shape, jnp.float32)
        for shift in range(1, n_ctx):
            pairs = [(i, i + shift) for i in range(n_ctx - shift)]
            prefix_f32 = prefix_f32 + lax.ppermute(state_bf, "ctx", pairs).astype(jnp.float32)
        prefix_state = prefix_f32.astype(jnp.bfloat16)

        scores = jnp.einsum("thd,shd->hts", q_heads, k_heads, preferred_element_type=jnp.float32)
        causal = jnp.arange(tok_rows)[:, None] >= jnp.arange(tok_rows)[None, :]
        scores = jnp.where(causal, scores, 0.0).astype(jnp.bfloat16)
        intra = jnp.einsum("hts,shd->thd", scores, v_heads, preferred_element_type=jnp.float32)
        inter = jnp.einsum("thd,hde->the", q_heads, prefix_state, preferred_element_type=jnp.float32)
        attn = (intra + inter).reshape(tok_rows, HEADS * HEAD_DIM)
        mean_sq = jnp.mean(attn * attn, axis=-1, keepdims=True)
        normed = (attn * lax.rsqrt(mean_sq + 1e-05) * norm_gain).astype(jnp.bfloat16)

        outs = [jnp.dot(normed, weight_block, preferred_element_type=jnp.float32)]
        for shift in range(1, n_ctx):
            pairs = [(i, (i - shift) % n_ctx) for i in range(n_ctx)]
            got = lax.ppermute(normed, "ctx", pairs)
            outs.append(jnp.dot(got, weight_block, preferred_element_type=jnp.float32))
        stacked = jnp.concatenate(outs + outs, axis=0).astype(jnp.bfloat16)
        position = lax.axis_index("ctx")
        return lax.dynamic_slice_in_dim(stacked, (n_ctx - position) * tok_rows, n_ctx * tok_rows, axis=0)

    return on_device


def solution(mesh):
    n_fsdp, n_ctx = mesh.devices.shape
    n_core = 2
    split = Mesh(mesh.devices.reshape(n_fsdp // n_core, n_core, n_ctx), ("chips", "core", "ctx"))
    rows = ("chips", "core", "ctx")
    placed = (
        P(rows, None),
        P(rows, None),
        P(rows, None),
        P(),
        P(("chips", "core"), "ctx"),
    )
    return jax.shard_map(
        make_on_device(n_ctx, n_core),
        mesh=split,
        in_specs=placed,
        out_specs=P(("chips", "core"), "ctx"),
        check_vma=False,
    )
```

```python
import jax
import jax.numpy as jnp
import numpy as np
from jax import lax
from jax.sharding import Mesh
from jax.sharding import PartitionSpec as P

HEADS = 32
HEAD_DIM = 96


def make_on_device(n_ctx, n_core):
    def on_device(queries, keys, values, norm_gain, out_weight):
        weight_block = out_weight
        for axis in ("core", "z", "y"):
            weight_block = lax.all_gather(weight_block, axis, axis=0, tiled=True)

        tok_rows = queries.shape[0]
        q_heads = queries.reshape(tok_rows, HEADS, HEAD_DIM)
        k_heads = keys.reshape(tok_rows, HEADS, HEAD_DIM)
        v_heads = values.reshape(tok_rows, HEADS, HEAD_DIM)
        local_state = jnp.einsum("shd,she->hde", k_heads, v_heads, preferred_element_type=jnp.float32)
        state_bf = local_state.astype(jnp.bfloat16)
        prefix_f32 = jnp.zeros(local_state.shape, jnp.float32)
        for shift in range(1, n_ctx):
            pairs = [(i, i + shift) for i in range(n_ctx - shift)]
            prefix_f32 = prefix_f32 + lax.ppermute(state_bf, "ctx", pairs).astype(jnp.float32)
        prefix_state = prefix_f32.astype(jnp.bfloat16)

        scores = jnp.einsum("thd,shd->hts", q_heads, k_heads, preferred_element_type=jnp.float32)
        causal = jnp.arange(tok_rows)[:, None] >= jnp.arange(tok_rows)[None, :]
        scores = jnp.where(causal, scores, 0.0).astype(jnp.bfloat16)
        intra = jnp.einsum("hts,shd->thd", scores, v_heads, preferred_element_type=jnp.float32)
        inter = jnp.einsum("thd,hde->the", q_heads, prefix_state, preferred_element_type=jnp.float32)
        attn = (intra + inter).reshape(tok_rows, HEADS * HEAD_DIM)
        mean_sq = jnp.mean(attn * attn, axis=-1, keepdims=True)
        normed = (attn * lax.rsqrt(mean_sq + 1e-05) * norm_gain).astype(jnp.bfloat16)

        outs = [jnp.dot(normed, weight_block, preferred_element_type=jnp.float32)]
        for shift in range(1, n_ctx):
            pairs = [(i, (i - shift) % n_ctx) for i in range(n_ctx)]
            got = lax.ppermute(normed, "ctx", pairs)
            outs.append(jnp.dot(got, weight_block, preferred_element_type=jnp.float32))
        stacked = jnp.concatenate(outs + outs, axis=0).astype(jnp.bfloat16)
        position = lax.axis_index("ctx")
        return lax.dynamic_slice_in_dim(stacked, (n_ctx - position) * tok_rows, n_ctx * tok_rows, axis=0)

    return on_device


def solution(mesh):
    n_fsdp, n_ctx = mesh.devices.shape
    n_core = 2
    n_y = len({d.coords[1] for d in mesh.devices.flat})
    n_z = n_fsdp // (n_core * n_y)
    split = Mesh(mesh.devices.reshape(n_y, n_z, n_core, n_ctx), ("y", "z", "core", "ctx"))
    rows = ("y", "z", "core", "ctx")
    placed = (
        P(rows, None),
        P(rows, None),
        P(rows, None),
        P(),
        P(("y", "z", "core"), "ctx"),
    )
    return jax.shard_map(
        make_on_device(n_ctx, n_core),
        mesh=split,
        in_specs=placed,
        out_specs=P(("y", "z", "core"), "ctx"),
        check_vma=False,
    )
```

```python
import jax
import jax.numpy as jnp
import numpy as np
from jax import lax
from jax.sharding import Mesh
from jax.sharding import PartitionSpec as P

HEADS = 32
HEAD_DIM = 96


def make_on_device(n_ctx, n_core):
    def on_device(queries, keys, values, norm_gain, out_weight):
        weight_block = out_weight
        for axis in ("core", "z", "y"):
            weight_block = lax.all_gather(weight_block, axis, axis=0, tiled=True)

        tok_rows = queries.shape[0]
        q_heads = queries.reshape(tok_rows, HEADS, HEAD_DIM)
        k_heads = keys.reshape(tok_rows, HEADS, HEAD_DIM)
        v_heads = values.reshape(tok_rows, HEADS, HEAD_DIM)
        local_state = jnp.einsum("shd,she->hde", k_heads, v_heads, preferred_element_type=jnp.float32)
        state_bf = local_state.astype(jnp.bfloat16)
        prefix_f32 = jnp.zeros(local_state.shape, jnp.float32)
        if n_ctx == 4:
            from_prev = lax.ppermute(state_bf, "ctx", [(0, 1), (1, 2), (2, 3)])
            from_first = lax.ppermute(state_bf, "ctx", [(0, 3)])
            forwarded = lax.ppermute(from_prev, "ctx", [(1, 2), (2, 3)])
            for got in (from_prev, from_first, forwarded):
                prefix_f32 = prefix_f32 + got.astype(jnp.float32)
        else:
            for shift in range(1, n_ctx):
                pairs = [(i, i + shift) for i in range(n_ctx - shift)]
                prefix_f32 = prefix_f32 + lax.ppermute(state_bf, "ctx", pairs).astype(jnp.float32)
        prefix_state = prefix_f32.astype(jnp.bfloat16)

        scores = jnp.einsum("thd,shd->hts", q_heads, k_heads, preferred_element_type=jnp.float32)
        causal = jnp.arange(tok_rows)[:, None] >= jnp.arange(tok_rows)[None, :]
        scores = jnp.where(causal, scores, 0.0).astype(jnp.bfloat16)
        intra = jnp.einsum("hts,shd->thd", scores, v_heads, preferred_element_type=jnp.float32)
        inter = jnp.einsum("thd,hde->the", q_heads, prefix_state, preferred_element_type=jnp.float32)
        attn = (intra + inter).reshape(tok_rows, HEADS * HEAD_DIM)
        mean_sq = jnp.mean(attn * attn, axis=-1, keepdims=True)
        normed = (attn * lax.rsqrt(mean_sq + 1e-05) * norm_gain).astype(jnp.bfloat16)

        def shift_by(x, s):
            return lax.ppermute(x, "ctx", [(i, (i - s) % n_ctx) for i in range(n_ctx)])

        half = HEADS * HEAD_DIM // 2
        outs = [None] * n_ctx
        outs[0] = jnp.dot(normed, weight_block, preferred_element_type=jnp.float32)
        ahead, behind = normed, normed
        for s in range(1, n_ctx // 2 + 1):
            if 2 * s < n_ctx:
                ahead = shift_by(ahead, 1)
                behind = shift_by(behind, -1)
                outs[s] = jnp.dot(ahead, weight_block, preferred_element_type=jnp.float32)
                outs[n_ctx - s] = jnp.dot(behind, weight_block, preferred_element_type=jnp.float32)
            else:
                left = shift_by(ahead[:, :half], 1)
                right = shift_by(behind[:, half:], -1)
                outs[s] = jnp.dot(left, weight_block[:half], preferred_element_type=jnp.float32) + jnp.dot(
                    right, weight_block[half:], preferred_element_type=jnp.float32
                )
        stacked = jnp.concatenate(outs + outs, axis=0).astype(jnp.bfloat16)
        position = lax.axis_index("ctx")
        return lax.dynamic_slice_in_dim(stacked, (n_ctx - position) * tok_rows, n_ctx * tok_rows, axis=0)

    return on_device


def solution(mesh):
    n_fsdp, n_ctx = mesh.devices.shape
    n_core = 2
    n_y = len({d.coords[1] for d in mesh.devices.flat})
    n_z = n_fsdp // (n_core * n_y)
    split = Mesh(mesh.devices.reshape(n_y, n_z, n_core, n_ctx), ("y", "z", "core", "ctx"))
    rows = ("y", "z", "core", "ctx")
    placed = (
        P(rows, None),
        P(rows, None),
        P(rows, None),
        P(),
        P(("y", "z", "core"), "ctx"),
    )
    return jax.shard_map(
        make_on_device(n_ctx, n_core),
        mesh=split,
        in_specs=placed,
        out_specs=P(("y", "z", "core"), "ctx"),
        check_vma=False,
    )
```

```python
import jax
import jax.numpy as jnp
import numpy as np
from jax import lax
from jax.sharding import Mesh
from jax.sharding import PartitionSpec as P

HEADS = 32
HEAD_DIM = 96


def make_on_device(n_ctx, n_core, n_y, n_z):
    def on_device(queries, keys, values, norm_gain, out_weight):
        rows, cols = out_weight.shape
        half = out_weight
        for axis in ("z", "y"):
            half = lax.all_gather(half, axis, axis=0, tiled=True)

        tok_rows = queries.shape[0]
        q_heads = queries.reshape(tok_rows, HEADS, HEAD_DIM)
        k_heads = keys.reshape(tok_rows, HEADS, HEAD_DIM)
        v_heads = values.reshape(tok_rows, HEADS, HEAD_DIM)
        local_state = jnp.einsum("shd,she->hde", k_heads, v_heads, preferred_element_type=jnp.float32)
        state_bf = local_state.astype(jnp.bfloat16)
        prefix_f32 = jnp.zeros(local_state.shape, jnp.float32)
        if n_ctx == 4:
            from_prev = lax.ppermute(state_bf, "ctx", [(0, 1), (1, 2), (2, 3)])
            from_first = lax.ppermute(state_bf, "ctx", [(0, 3)])
            forwarded = lax.ppermute(from_prev, "ctx", [(1, 2), (2, 3)])
            for got in (from_prev, from_first, forwarded):
                prefix_f32 = prefix_f32 + got.astype(jnp.float32)
        else:
            for shift in range(1, n_ctx):
                pairs = [(i, i + shift) for i in range(n_ctx - shift)]
                prefix_f32 = prefix_f32 + lax.ppermute(state_bf, "ctx", pairs).astype(jnp.float32)
        prefix_state = prefix_f32.astype(jnp.bfloat16)

        half, _ = lax.optimization_barrier((half, prefix_f32))
        other = lax.ppermute(half, "core", [(0, 1), (1, 0)])
        mine_first = lax.axis_index("core") == 0
        half = half.reshape(-1, 1, rows, cols)
        other = other.reshape(-1, 1, rows, cols)
        weight_block = jnp.concatenate(
            [jnp.where(mine_first, half, other), jnp.where(mine_first, other, half)], axis=1
        ).reshape(-1, cols)

        scores = jnp.einsum("thd,shd->hts", q_heads, k_heads, preferred_element_type=jnp.float32)
        causal = jnp.arange(tok_rows)[:, None] >= jnp.arange(tok_rows)[None, :]
        scores = jnp.where(causal, scores, 0.0).astype(jnp.bfloat16)
        intra = jnp.einsum("hts,shd->thd", scores, v_heads, preferred_element_type=jnp.float32)
        inter = jnp.einsum("thd,hde->the", q_heads, prefix_state, preferred_element_type=jnp.float32)
        attn = (intra + inter).reshape(tok_rows, HEADS * HEAD_DIM)
        mean_sq = jnp.mean(attn * attn, axis=-1, keepdims=True)
        normed = (attn * lax.rsqrt(mean_sq + 1e-05) * norm_gain).astype(jnp.bfloat16)

        def shift_by(x, s):
            return lax.ppermute(x, "ctx", [(i, (i - s) % n_ctx) for i in range(n_ctx)])

        half = HEADS * HEAD_DIM // 2
        outs = [None] * n_ctx
        outs[0] = jnp.dot(normed, weight_block, preferred_element_type=jnp.float32)
        ahead, behind = normed, normed
        for s in range(1, n_ctx // 2 + 1):
            if 2 * s < n_ctx:
                ahead = shift_by(ahead, 1)
                behind = shift_by(behind, -1)
                outs[s] = jnp.dot(ahead, weight_block, preferred_element_type=jnp.float32)
                outs[n_ctx - s] = jnp.dot(behind, weight_block, preferred_element_type=jnp.float32)
            else:
                left = shift_by(ahead[:, :half], 1)
                right = shift_by(behind[:, half:], -1)
                outs[s] = jnp.dot(left, weight_block[:half], preferred_element_type=jnp.float32) + jnp.dot(
                    right, weight_block[half:], preferred_element_type=jnp.float32
                )
        stacked = jnp.concatenate(outs + outs, axis=0).astype(jnp.bfloat16)
        position = lax.axis_index("ctx")
        return lax.dynamic_slice_in_dim(stacked, (n_ctx - position) * tok_rows, n_ctx * tok_rows, axis=0)

    return on_device


def solution(mesh):
    n_fsdp, n_ctx = mesh.devices.shape
    n_core = 2
    n_y = len({d.coords[1] for d in mesh.devices.flat})
    n_z = n_fsdp // (n_core * n_y)
    split = Mesh(mesh.devices.reshape(n_y, n_z, n_core, n_ctx), ("y", "z", "core", "ctx"))
    rows = ("y", "z", "core", "ctx")
    placed = (
        P(rows, None),
        P(rows, None),
        P(rows, None),
        P(),
        P(("y", "z", "core"), "ctx"),
    )
    return jax.shard_map(
        make_on_device(n_ctx, n_core, n_y, n_z),
        mesh=split,
        in_specs=placed,
        out_specs=P(("y", "z", "core"), "ctx"),
        check_vma=False,
    )
```

```python
import jax
import jax.numpy as jnp
import numpy as np
from jax import lax
from jax.sharding import Mesh
from jax.sharding import PartitionSpec as P

HEADS = 32
HEAD_DIM = 96


def make_on_device(n_ctx, n_core, n_y, n_z):
    def on_device(queries, keys, values, norm_gain, out_weight):
        rows, cols = out_weight.shape
        half = out_weight
        for axis in ("y", "z"):
            half = lax.all_gather(half, axis, axis=0, tiled=True)

        tok_rows = queries.shape[0]
        q_heads = queries.reshape(tok_rows, HEADS, HEAD_DIM)
        k_heads = keys.reshape(tok_rows, HEADS, HEAD_DIM)
        v_heads = values.reshape(tok_rows, HEADS, HEAD_DIM)
        local_state = jnp.einsum("shd,she->hde", k_heads, v_heads, preferred_element_type=jnp.float32)
        state_bf = local_state.astype(jnp.bfloat16)
        prefix_f32 = jnp.zeros(local_state.shape, jnp.float32)
        if n_ctx == 4:
            from_prev = lax.ppermute(state_bf, "ctx", [(0, 1), (1, 2), (2, 3)])
            from_first = lax.ppermute(state_bf, "ctx", [(0, 3)])
            forwarded = lax.ppermute(from_prev, "ctx", [(1, 2), (2, 3)])
            for got in (from_prev, from_first, forwarded):
                prefix_f32 = prefix_f32 + got.astype(jnp.float32)
        else:
            for shift in range(1, n_ctx):
                pairs = [(i, i + shift) for i in range(n_ctx - shift)]
                prefix_f32 = prefix_f32 + lax.ppermute(state_bf, "ctx", pairs).astype(jnp.float32)
        prefix_state = prefix_f32.astype(jnp.bfloat16)


        scores = jnp.einsum("thd,shd->hts", q_heads, k_heads, preferred_element_type=jnp.float32)
        causal = jnp.arange(tok_rows)[:, None] >= jnp.arange(tok_rows)[None, :]
        scores = jnp.where(causal, scores, 0.0).astype(jnp.bfloat16)
        intra = jnp.einsum("hts,shd->thd", scores, v_heads, preferred_element_type=jnp.float32)
        inter = jnp.einsum("thd,hde->the", q_heads, prefix_state, preferred_element_type=jnp.float32)
        attn = (intra + inter).reshape(tok_rows, HEADS * HEAD_DIM)
        mean_sq = jnp.mean(attn * attn, axis=-1, keepdims=True)
        normed = (attn * lax.rsqrt(mean_sq + 1e-05) * norm_gain).astype(jnp.bfloat16)

        half, _ = lax.optimization_barrier((half, normed))
        other = lax.ppermute(half, "core", [(0, 1), (1, 0)])
        mine_first = lax.axis_index("core") == 0

        def fsdp_order(h):
            return h.reshape(n_z, n_y, 1, rows, cols).transpose(1, 0, 2, 3, 4)

        half, other = fsdp_order(half), fsdp_order(other)
        weight_block = jnp.concatenate(
            [jnp.where(mine_first, half, other), jnp.where(mine_first, other, half)], axis=2
        ).reshape(-1, cols)

        def shift_by(x, s):
            return lax.ppermute(x, "ctx", [(i, (i - s) % n_ctx) for i in range(n_ctx)])

        half = HEADS * HEAD_DIM // 2
        outs = [None] * n_ctx
        outs[0] = jnp.dot(normed, weight_block, preferred_element_type=jnp.float32)
        ahead, behind = normed, normed
        for s in range(1, n_ctx // 2 + 1):
            if 2 * s < n_ctx:
                ahead = shift_by(ahead, 1)
                behind = shift_by(behind, -1)
                outs[s] = jnp.dot(ahead, weight_block, preferred_element_type=jnp.float32)
                outs[n_ctx - s] = jnp.dot(behind, weight_block, preferred_element_type=jnp.float32)
            else:
                left = shift_by(ahead[:, :half], 1)
                right = shift_by(behind[:, half:], -1)
                outs[s] = jnp.dot(left, weight_block[:half], preferred_element_type=jnp.float32) + jnp.dot(
                    right, weight_block[half:], preferred_element_type=jnp.float32
                )
        stacked = jnp.concatenate(outs + outs, axis=0).astype(jnp.bfloat16)
        position = lax.axis_index("ctx")
        return lax.dynamic_slice_in_dim(stacked, (n_ctx - position) * tok_rows, n_ctx * tok_rows, axis=0)

    return on_device


def solution(mesh):
    n_fsdp, n_ctx = mesh.devices.shape
    n_core = 2
    n_y = len({d.coords[1] for d in mesh.devices.flat})
    n_z = n_fsdp // (n_core * n_y)
    split = Mesh(mesh.devices.reshape(n_y, n_z, n_core, n_ctx), ("y", "z", "core", "ctx"))
    rows = ("y", "z", "core", "ctx")
    placed = (
        P(rows, None),
        P(rows, None),
        P(rows, None),
        P(),
        P(("y", "z", "core"), "ctx"),
    )
    return jax.shard_map(
        make_on_device(n_ctx, n_core, n_y, n_z),
        mesh=split,
        in_specs=placed,
        out_specs=P(("y", "z", "core"), "ctx"),
        check_vma=False,
    )
```

```python
import jax
import jax.numpy as jnp
import numpy as np
from jax import lax
from jax.sharding import Mesh
from jax.sharding import PartitionSpec as P

HEADS = 32
HEAD_DIM = 96


def make_on_device(n_ctx, n_core):
    def on_device(queries, keys, values, norm_gain, out_weight):
        weight_block = out_weight
        for axis in ("core", "z", "y"):
            weight_block = lax.all_gather(weight_block, axis, axis=0, tiled=True)

        tok_rows = queries.shape[0]
        q_heads = queries.reshape(tok_rows, HEADS, HEAD_DIM)
        k_heads = keys.reshape(tok_rows, HEADS, HEAD_DIM)
        v_heads = values.reshape(tok_rows, HEADS, HEAD_DIM)
        local_state = jnp.einsum("shd,she->hde", k_heads, v_heads, preferred_element_type=jnp.float32)
        state_bf = local_state.astype(jnp.bfloat16)
        prefix_f32 = jnp.zeros(local_state.shape, jnp.float32)
        if n_ctx == 4:
            from_prev = lax.ppermute(state_bf, "ctx", [(0, 1), (1, 2), (2, 3)])
            from_first = lax.ppermute(state_bf, "ctx", [(0, 3)])
            forwarded = lax.ppermute(from_prev, "ctx", [(1, 2), (2, 3)])
            for got in (from_prev, from_first, forwarded):
                prefix_f32 = prefix_f32 + got.astype(jnp.float32)
        else:
            for shift in range(1, n_ctx):
                pairs = [(i, i + shift) for i in range(n_ctx - shift)]
                prefix_f32 = prefix_f32 + lax.ppermute(state_bf, "ctx", pairs).astype(jnp.float32)
        prefix_state = prefix_f32.astype(jnp.bfloat16)

        scores = jnp.einsum("thd,shd->hts", q_heads, k_heads, preferred_element_type=jnp.float32)
        causal = jnp.arange(tok_rows)[:, None] >= jnp.arange(tok_rows)[None, :]
        scores = jnp.where(causal, scores, 0.0).astype(jnp.bfloat16)
        intra = jnp.einsum("hts,shd->thd", scores, v_heads, preferred_element_type=jnp.float32)
        inter = jnp.einsum("thd,hde->the", q_heads, prefix_state, preferred_element_type=jnp.float32)
        attn = (intra + inter).reshape(tok_rows, HEADS * HEAD_DIM)
        mean_sq = jnp.mean(attn * attn, axis=-1, keepdims=True)
        normed = (attn * lax.rsqrt(mean_sq + 1e-05) * norm_gain).astype(jnp.bfloat16)

        def shift_by(x, s):
            return lax.ppermute(x, "ctx", [(i, (i - s) % n_ctx) for i in range(n_ctx)])

        position = lax.axis_index("ctx")

        def place(seq, block, s, col=0):
            row = ((position + s) % n_ctx) * tok_rows
            return lax.dynamic_update_slice(seq, block, (row, col))

        half = HEADS * HEAD_DIM // 2
        seq = place(jnp.zeros((n_ctx * tok_rows, HEADS * HEAD_DIM), jnp.bfloat16), normed, 0)
        ahead, behind = normed, normed
        for s in range(1, n_ctx // 2 + 1):
            if 2 * s < n_ctx:
                ahead = shift_by(ahead, 1)
                behind = shift_by(behind, -1)
                seq = place(place(seq, ahead, s), behind, n_ctx - s)
            else:
                seq = place(seq, shift_by(ahead[:, :half], 1), s)
                seq = place(seq, shift_by(behind[:, half:], -1), s, half)
        return jnp.dot(seq, weight_block, preferred_element_type=jnp.float32).astype(jnp.bfloat16)

    return on_device


def solution(mesh):
    n_fsdp, n_ctx = mesh.devices.shape
    n_core = 2
    n_y = len({d.coords[1] for d in mesh.devices.flat})
    n_z = n_fsdp // (n_core * n_y)
    split = Mesh(mesh.devices.reshape(n_y, n_z, n_core, n_ctx), ("y", "z", "core", "ctx"))
    rows = ("y", "z", "core", "ctx")
    placed = (
        P(rows, None),
        P(rows, None),
        P(rows, None),
        P(),
        P(("y", "z", "core"), "ctx"),
    )
    return jax.shard_map(
        make_on_device(n_ctx, n_core),
        mesh=split,
        in_specs=placed,
        out_specs=P(("y", "z", "core"), "ctx"),
        check_vma=False,
    )
```

```python
import jax
import jax.numpy as jnp
import numpy as np
from jax import lax
from jax.sharding import Mesh
from jax.sharding import PartitionSpec as P

HEADS = 32
HEAD_DIM = 96


def make_on_device(n_ctx, n_core, n_y, n_z):
    def on_device(queries, keys, values, norm_gain, out_weight):
        rows, cols = out_weight.shape
        w_mine = out_weight
        for axis in ("z", "y"):
            w_mine = lax.all_gather(w_mine, axis, axis=0, tiled=True)

        tok_rows = queries.shape[0]
        q_heads = queries.reshape(tok_rows, HEADS, HEAD_DIM)
        k_heads = keys.reshape(tok_rows, HEADS, HEAD_DIM)
        v_heads = values.reshape(tok_rows, HEADS, HEAD_DIM)
        local_state = jnp.einsum("shd,she->hde", k_heads, v_heads, preferred_element_type=jnp.float32)
        state_bf = local_state.astype(jnp.bfloat16)
        prefix_f32 = jnp.zeros(local_state.shape, jnp.float32)
        if n_ctx == 4:
            from_prev = lax.ppermute(state_bf, "ctx", [(0, 1), (1, 2), (2, 3)])
            from_first = lax.ppermute(state_bf, "ctx", [(0, 3)])
            forwarded = lax.ppermute(from_prev, "ctx", [(1, 2), (2, 3)])
            for got in (from_prev, from_first, forwarded):
                prefix_f32 = prefix_f32 + got.astype(jnp.float32)
        else:
            for shift in range(1, n_ctx):
                pairs = [(i, i + shift) for i in range(n_ctx - shift)]
                prefix_f32 = prefix_f32 + lax.ppermute(state_bf, "ctx", pairs).astype(jnp.float32)
        prefix_state = prefix_f32.astype(jnp.bfloat16)

        scores = jnp.einsum("thd,shd->hts", q_heads, k_heads, preferred_element_type=jnp.float32)
        causal = jnp.arange(tok_rows)[:, None] >= jnp.arange(tok_rows)[None, :]
        scores = jnp.where(causal, scores, 0.0).astype(jnp.bfloat16)
        intra = jnp.einsum("hts,shd->thd", scores, v_heads, preferred_element_type=jnp.float32)
        inter = jnp.einsum("thd,hde->the", q_heads, prefix_state, preferred_element_type=jnp.float32)
        attn = (intra + inter).reshape(tok_rows, HEADS * HEAD_DIM)
        mean_sq = jnp.mean(attn * attn, axis=-1, keepdims=True)
        normed = (attn * lax.rsqrt(mean_sq + 1e-05) * norm_gain).astype(jnp.bfloat16)

        def shift_by(x, s):
            return lax.ppermute(x, "ctx", [(i, (i - s) % n_ctx) for i in range(n_ctx)])

        half = HEADS * HEAD_DIM // 2
        outs = [None] * n_ctx
        ahead, behind = normed, normed
        received = [normed] + [None] * (n_ctx - 1)
        for s in range(1, n_ctx // 2 + 1):
            if 2 * s < n_ctx:
                ahead = shift_by(ahead, 1)
                behind = shift_by(behind, -1)
                received[s], received[n_ctx - s] = ahead, behind
            else:
                received[s] = (shift_by(ahead[:, :half], 1), shift_by(behind[:, half:], -1))
            if s == 1:
                w_mine, _, _ = lax.optimization_barrier((w_mine, ahead, behind))
                w_other = lax.ppermute(w_mine, "core", [(0, 1), (1, 0)])
                mine_first = lax.axis_index("core") == 0
                w_mine = w_mine.reshape(-1, 1, rows, cols)
                w_other = w_other.reshape(-1, 1, rows, cols)
                weight_block = jnp.concatenate(
                    [jnp.where(mine_first, w_mine, w_other), jnp.where(mine_first, w_other, w_mine)], axis=1
                ).reshape(-1, cols)
        for s in range(n_ctx):
            if isinstance(received[s], tuple):
                left, right = received[s]
                outs[s] = jnp.dot(left, weight_block[:half], preferred_element_type=jnp.float32) + jnp.dot(
                    right, weight_block[half:], preferred_element_type=jnp.float32
                )
            else:
                outs[s] = jnp.dot(received[s], weight_block, preferred_element_type=jnp.float32)
        stacked = jnp.concatenate(outs + outs, axis=0).astype(jnp.bfloat16)
        position = lax.axis_index("ctx")
        return lax.dynamic_slice_in_dim(stacked, (n_ctx - position) * tok_rows, n_ctx * tok_rows, axis=0)

    return on_device


def solution(mesh):
    n_fsdp, n_ctx = mesh.devices.shape
    n_core = 2
    n_y = len({d.coords[1] for d in mesh.devices.flat})
    n_z = n_fsdp // (n_core * n_y)
    split = Mesh(mesh.devices.reshape(n_y, n_z, n_core, n_ctx), ("y", "z", "core", "ctx"))
    rows = ("y", "z", "core", "ctx")
    placed = (
        P(rows, None),
        P(rows, None),
        P(rows, None),
        P(),
        P(("y", "z", "core"), "ctx"),
    )
    return jax.shard_map(
        make_on_device(n_ctx, n_core, n_y, n_z),
        mesh=split,
        in_specs=placed,
        out_specs=P(("y", "z", "core"), "ctx"),
        check_vma=False,
    )
```

```python
import jax
import jax.numpy as jnp
import numpy as np
from jax import lax
from jax.sharding import Mesh
from jax.sharding import PartitionSpec as P

HEADS = 32
HEAD_DIM = 96


def make_on_device(n_ctx, n_core):
    def on_device(queries, keys, values, norm_gain, out_weight):
        weight_block = out_weight
        for axis in (("z", "core"), "y"):
            weight_block = lax.all_gather(weight_block, axis, axis=0, tiled=True)

        tok_rows = queries.shape[0]
        q_heads = queries.reshape(tok_rows, HEADS, HEAD_DIM)
        k_heads = keys.reshape(tok_rows, HEADS, HEAD_DIM)
        v_heads = values.reshape(tok_rows, HEADS, HEAD_DIM)
        local_state = jnp.einsum("shd,she->hde", k_heads, v_heads, preferred_element_type=jnp.float32)
        state_bf = local_state.astype(jnp.bfloat16)
        prefix_f32 = jnp.zeros(local_state.shape, jnp.float32)
        if n_ctx == 4:
            from_prev = lax.ppermute(state_bf, "ctx", [(0, 1), (1, 2), (2, 3)])
            from_first = lax.ppermute(state_bf, "ctx", [(0, 3)])
            forwarded = lax.ppermute(from_prev, "ctx", [(1, 2), (2, 3)])
            for got in (from_prev, from_first, forwarded):
                prefix_f32 = prefix_f32 + got.astype(jnp.float32)
        else:
            for shift in range(1, n_ctx):
                pairs = [(i, i + shift) for i in range(n_ctx - shift)]
                prefix_f32 = prefix_f32 + lax.ppermute(state_bf, "ctx", pairs).astype(jnp.float32)
        prefix_state = prefix_f32.astype(jnp.bfloat16)

        scores = jnp.einsum("thd,shd->hts", q_heads, k_heads, preferred_element_type=jnp.float32)
        causal = jnp.arange(tok_rows)[:, None] >= jnp.arange(tok_rows)[None, :]
        scores = jnp.where(causal, scores, 0.0).astype(jnp.bfloat16)
        intra = jnp.einsum("hts,shd->thd", scores, v_heads, preferred_element_type=jnp.float32)
        inter = jnp.einsum("thd,hde->the", q_heads, prefix_state, preferred_element_type=jnp.float32)
        attn = (intra + inter).reshape(tok_rows, HEADS * HEAD_DIM)
        mean_sq = jnp.mean(attn * attn, axis=-1, keepdims=True)
        normed = (attn * lax.rsqrt(mean_sq + 1e-05) * norm_gain).astype(jnp.bfloat16)

        def shift_by(x, s):
            return lax.ppermute(x, "ctx", [(i, (i - s) % n_ctx) for i in range(n_ctx)])

        half = HEADS * HEAD_DIM // 2
        outs = [None] * n_ctx
        outs[0] = jnp.dot(normed, weight_block, preferred_element_type=jnp.float32)
        ahead, behind = normed, normed
        for s in range(1, n_ctx // 2 + 1):
            if 2 * s < n_ctx:
                ahead = shift_by(ahead, 1)
                behind = shift_by(behind, -1)
                outs[s] = jnp.dot(ahead, weight_block, preferred_element_type=jnp.float32)
                outs[n_ctx - s] = jnp.dot(behind, weight_block, preferred_element_type=jnp.float32)
            else:
                left = shift_by(ahead[:, :half], 1)
                right = shift_by(behind[:, half:], -1)
                outs[s] = jnp.dot(left, weight_block[:half], preferred_element_type=jnp.float32) + jnp.dot(
                    right, weight_block[half:], preferred_element_type=jnp.float32
                )
        stacked = jnp.concatenate(outs + outs, axis=0).astype(jnp.bfloat16)
        position = lax.axis_index("ctx")
        return lax.dynamic_slice_in_dim(stacked, (n_ctx - position) * tok_rows, n_ctx * tok_rows, axis=0)

    return on_device


def solution(mesh):
    n_fsdp, n_ctx = mesh.devices.shape
    n_core = 2
    n_y = len({d.coords[1] for d in mesh.devices.flat})
    n_z = n_fsdp // (n_core * n_y)
    split = Mesh(mesh.devices.reshape(n_y, n_z, n_core, n_ctx), ("y", "z", "core", "ctx"))
    rows = ("y", "z", "core", "ctx")
    placed = (
        P(rows, None),
        P(rows, None),
        P(rows, None),
        P(),
        P(("y", "z", "core"), "ctx"),
    )
    return jax.shard_map(
        make_on_device(n_ctx, n_core),
        mesh=split,
        in_specs=placed,
        out_specs=P(("y", "z", "core"), "ctx"),
        check_vma=False,
    )
```

```python
import jax
import jax.numpy as jnp
import numpy as np
from jax import lax
from jax.sharding import Mesh
from jax.sharding import PartitionSpec as P

HEADS = 32
HEAD_DIM = 96


def make_on_device(n_ctx, n_core):
    def on_device(queries, keys, values, norm_gain, out_weight):
        weight_block = out_weight
        for axis in ("core", "z", "y"):
            weight_block = lax.all_gather(weight_block, axis, axis=0, tiled=True)

        tok_rows = queries.shape[0]
        q_heads = queries.reshape(tok_rows, HEADS, HEAD_DIM)
        k_heads = keys.reshape(tok_rows, HEADS, HEAD_DIM)
        v_heads = values.reshape(tok_rows, HEADS, HEAD_DIM)
        local_state = jnp.einsum("shd,she->hde", k_heads, v_heads, preferred_element_type=jnp.float32)
        state_bf = local_state.astype(jnp.bfloat16)
        prefix_f32 = jnp.zeros(local_state.shape, jnp.float32)
        if n_ctx == 4:
            from_prev = lax.ppermute(state_bf, "ctx", [(0, 1), (1, 2), (2, 3)])
            from_first = lax.ppermute(state_bf, "ctx", [(0, 3)])
            forwarded = lax.ppermute(from_prev, "ctx", [(1, 2), (2, 3)])
            for got in (from_prev, from_first, forwarded):
                prefix_f32 = prefix_f32 + got.astype(jnp.float32)
        else:
            for shift in range(1, n_ctx):
                pairs = [(i, i + shift) for i in range(n_ctx - shift)]
                prefix_f32 = prefix_f32 + lax.ppermute(state_bf, "ctx", pairs).astype(jnp.float32)
        prefix_state = prefix_f32.astype(jnp.bfloat16)

        scores = jnp.einsum("thd,shd->hts", q_heads, k_heads, preferred_element_type=jnp.float32)
        causal = jnp.arange(tok_rows)[:, None] >= jnp.arange(tok_rows)[None, :]
        scores = jnp.where(causal, scores, 0.0).astype(jnp.bfloat16)
        intra = jnp.einsum("hts,shd->thd", scores, v_heads, preferred_element_type=jnp.float32)
        inter = jnp.einsum("thd,hde->the", q_heads, prefix_state, preferred_element_type=jnp.float32)
        attn = (intra + inter).reshape(tok_rows, HEADS * HEAD_DIM)
        mean_sq = jnp.mean(attn * attn, axis=-1, keepdims=True)
        normed = (attn * lax.rsqrt(mean_sq + 1e-05) * norm_gain).astype(jnp.bfloat16)

        def shift_by(x, s):
            return lax.ppermute(x, "ctx", [(i, (i - s) % n_ctx) for i in range(n_ctx)])

        half = HEADS * HEAD_DIM // 2
        position = lax.axis_index("ctx")
        cols = weight_block.shape[1]
        result = jnp.zeros((n_ctx * tok_rows, cols), jnp.bfloat16)

        def put(result, product, s):
            row = ((position + s) % n_ctx) * tok_rows
            return lax.dynamic_update_slice_in_dim(result, product.astype(jnp.bfloat16), row, axis=0)

        result = put(result, jnp.dot(normed, weight_block, preferred_element_type=jnp.float32), 0)
        ahead, behind = normed, normed
        for s in range(1, n_ctx // 2 + 1):
            if 2 * s < n_ctx:
                ahead = shift_by(ahead, 1)
                behind = shift_by(behind, -1)
                result = put(result, jnp.dot(ahead, weight_block, preferred_element_type=jnp.float32), s)
                result = put(result, jnp.dot(behind, weight_block, preferred_element_type=jnp.float32), n_ctx - s)
            else:
                left = shift_by(ahead[:, :half], 1)
                right = shift_by(behind[:, half:], -1)
                both = jnp.dot(left, weight_block[:half], preferred_element_type=jnp.float32) + jnp.dot(
                    right, weight_block[half:], preferred_element_type=jnp.float32
                )
                result = put(result, both, s)
        return result

    return on_device


def solution(mesh):
    n_fsdp, n_ctx = mesh.devices.shape
    n_core = 2
    n_y = len({d.coords[1] for d in mesh.devices.flat})
    n_z = n_fsdp // (n_core * n_y)
    split = Mesh(mesh.devices.reshape(n_y, n_z, n_core, n_ctx), ("y", "z", "core", "ctx"))
    rows = ("y", "z", "core", "ctx")
    placed = (
        P(rows, None),
        P(rows, None),
        P(rows, None),
        P(),
        P(("y", "z", "core"), "ctx"),
    )
    return jax.shard_map(
        make_on_device(n_ctx, n_core),
        mesh=split,
        in_specs=placed,
        out_specs=P(("y", "z", "core"), "ctx"),
        check_vma=False,
    )
```

```python
import jax
import jax.numpy as jnp
import numpy as np
from jax import lax
from jax.sharding import Mesh
from jax.sharding import PartitionSpec as P

HEADS = 32
HEAD_DIM = 96


def make_on_device(n_ctx, n_core):
    def on_device(queries, keys, values, norm_gain, out_weight):
        weight_block = out_weight
        for axis in ("core", "z", "y"):
            weight_block = lax.all_gather(weight_block, axis, axis=0, tiled=True)

        tok_rows = queries.shape[0]
        q_heads = queries.reshape(tok_rows, HEADS, HEAD_DIM)
        k_heads = keys.reshape(tok_rows, HEADS, HEAD_DIM)
        v_heads = values.reshape(tok_rows, HEADS, HEAD_DIM)
        local_state = jnp.einsum("shd,she->hde", k_heads, v_heads, preferred_element_type=jnp.float32)
        state_bf = local_state.astype(jnp.bfloat16)
        prefix_f32 = jnp.zeros(local_state.shape, jnp.float32)
        if n_ctx == 4:
            from_prev = lax.ppermute(state_bf, "ctx", [(0, 1), (1, 2), (2, 3)])
            from_first = lax.ppermute(state_bf, "ctx", [(0, 3)])
            forwarded = lax.ppermute(from_prev, "ctx", [(1, 2), (2, 3)])
            for got in (from_prev, from_first, forwarded):
                prefix_f32 = prefix_f32 + got.astype(jnp.float32)
        else:
            for shift in range(1, n_ctx):
                pairs = [(i, i + shift) for i in range(n_ctx - shift)]
                prefix_f32 = prefix_f32 + lax.ppermute(state_bf, "ctx", pairs).astype(jnp.float32)
        prefix_state = prefix_f32.astype(jnp.bfloat16)

        scores = jnp.einsum("thd,shd->hts", q_heads, k_heads, preferred_element_type=jnp.float32)
        causal = jnp.arange(tok_rows)[:, None] >= jnp.arange(tok_rows)[None, :]
        scores = jnp.where(causal, scores, 0.0).astype(jnp.bfloat16)
        intra = jnp.einsum("hts,shd->thd", scores, v_heads, preferred_element_type=jnp.float32)
        inter = jnp.einsum("thd,hde->the", q_heads, prefix_state, preferred_element_type=jnp.float32)
        attn = (intra + inter).reshape(tok_rows, HEADS * HEAD_DIM)
        mean_sq = jnp.mean(attn * attn, axis=-1, keepdims=True)
        normed = (attn * lax.rsqrt(mean_sq + 1e-05) * norm_gain).astype(jnp.bfloat16)

        def shift_by(x, s):
            return lax.ppermute(x, "ctx", [(i, (i - s) % n_ctx) for i in range(n_ctx)])

        half = HEADS * HEAD_DIM // 2
        position = lax.axis_index("ctx")
        cols = weight_block.shape[1]
        result = jnp.zeros((n_ctx * tok_rows, cols), jnp.bfloat16)

        def put(result, product, s):
            row = ((position + s) % n_ctx) * tok_rows
            return lax.dynamic_update_slice_in_dim(result, product.astype(jnp.bfloat16), row, axis=0)

        full = [(0, normed)]
        ahead, behind = normed, normed
        for s in range(1, n_ctx // 2 + 1):
            if 2 * s < n_ctx:
                ahead = shift_by(ahead, 1)
                behind = shift_by(behind, -1)
                full += [(s, ahead), (n_ctx - s, behind)]
            else:
                left = shift_by(ahead[:, :half], 1)
                right = shift_by(behind[:, half:], -1)
                both = jnp.dot(left, weight_block[:half], preferred_element_type=jnp.float32) + jnp.dot(
                    right, weight_block[half:], preferred_element_type=jnp.float32
                )
                result = put(result, both, s)
        products = jnp.dot(
            jnp.concatenate([block for _, block in full], axis=0), weight_block, preferred_element_type=jnp.float32
        )
        for i, (s, _) in enumerate(full):
            result = put(result, products[i * tok_rows:(i + 1) * tok_rows], s)
        return result

    return on_device


def solution(mesh):
    n_fsdp, n_ctx = mesh.devices.shape
    n_core = 2
    n_y = len({d.coords[1] for d in mesh.devices.flat})
    n_z = n_fsdp // (n_core * n_y)
    split = Mesh(mesh.devices.reshape(n_y, n_z, n_core, n_ctx), ("y", "z", "core", "ctx"))
    rows = ("y", "z", "core", "ctx")
    placed = (
        P(rows, None),
        P(rows, None),
        P(rows, None),
        P(),
        P(("y", "z", "core"), "ctx"),
    )
    return jax.shard_map(
        make_on_device(n_ctx, n_core),
        mesh=split,
        in_specs=placed,
        out_specs=P(("y", "z", "core"), "ctx"),
        check_vma=False,
    )
```

```python
import jax
import jax.numpy as jnp
import numpy as np
from jax import lax
from jax.sharding import Mesh
from jax.sharding import PartitionSpec as P

HEADS = 32
HEAD_DIM = 96


def make_on_device(n_ctx, n_core):
    def on_device(queries, keys, values, norm_gain, out_weight):
        weight_block = out_weight
        for axis in ("core", "z", "y"):
            weight_block = lax.all_gather(weight_block, axis, axis=0, tiled=True)

        tok_rows = queries.shape[0]
        q_heads = queries.reshape(tok_rows, HEADS, HEAD_DIM)
        k_heads = keys.reshape(tok_rows, HEADS, HEAD_DIM)
        v_heads = values.reshape(tok_rows, HEADS, HEAD_DIM)
        local_state = jnp.einsum("shd,she->hde", k_heads, v_heads, preferred_element_type=jnp.float32)
        state_bf = local_state.astype(jnp.bfloat16)
        scores = jnp.einsum("thd,shd->hts", q_heads, k_heads, preferred_element_type=jnp.float32)
        causal = jnp.arange(tok_rows)[:, None] >= jnp.arange(tok_rows)[None, :]
        scores = jnp.where(causal, scores, 0.0).astype(jnp.bfloat16)
        intra = jnp.einsum("hts,shd->thd", scores, v_heads, preferred_element_type=jnp.float32)
        prefix_f32 = jnp.zeros(local_state.shape, jnp.float32)
        if n_ctx == 4:
            from_prev = lax.ppermute(state_bf, "ctx", [(0, 1), (1, 2), (2, 3)])
            from_first = lax.ppermute(state_bf, "ctx", [(0, 3)])
            from_prev, intra = lax.optimization_barrier((from_prev, intra))
            forwarded = lax.ppermute(from_prev, "ctx", [(1, 2), (2, 3)])
            for got in (from_prev, from_first, forwarded):
                prefix_f32 = prefix_f32 + got.astype(jnp.float32)
        else:
            for shift in range(1, n_ctx):
                pairs = [(i, i + shift) for i in range(n_ctx - shift)]
                prefix_f32 = prefix_f32 + lax.ppermute(state_bf, "ctx", pairs).astype(jnp.float32)
        prefix_state = prefix_f32.astype(jnp.bfloat16)

        inter = jnp.einsum("thd,hde->the", q_heads, prefix_state, preferred_element_type=jnp.float32)
        attn = (intra + inter).reshape(tok_rows, HEADS * HEAD_DIM)
        mean_sq = jnp.mean(attn * attn, axis=-1, keepdims=True)
        normed = (attn * lax.rsqrt(mean_sq + 1e-05) * norm_gain).astype(jnp.bfloat16)

        def shift_by(x, s):
            return lax.ppermute(x, "ctx", [(i, (i - s) % n_ctx) for i in range(n_ctx)])

        half = HEADS * HEAD_DIM // 2
        position = lax.axis_index("ctx")
        cols = weight_block.shape[1]
        result = jnp.zeros((n_ctx * tok_rows, cols), jnp.bfloat16)

        def put(result, product, s):
            row = ((position + s) % n_ctx) * tok_rows
            return lax.dynamic_update_slice_in_dim(result, product.astype(jnp.bfloat16), row, axis=0)

        result = put(result, jnp.dot(normed, weight_block, preferred_element_type=jnp.float32), 0)
        ahead, behind = normed, normed
        for s in range(1, n_ctx // 2 + 1):
            if 2 * s < n_ctx:
                ahead = shift_by(ahead, 1)
                behind = shift_by(behind, -1)
                result = put(result, jnp.dot(ahead, weight_block, preferred_element_type=jnp.float32), s)
                result = put(result, jnp.dot(behind, weight_block, preferred_element_type=jnp.float32), n_ctx - s)
            else:
                left = shift_by(ahead[:, :half], 1)
                right = shift_by(behind[:, half:], -1)
                both = jnp.dot(left, weight_block[:half], preferred_element_type=jnp.float32) + jnp.dot(
                    right, weight_block[half:], preferred_element_type=jnp.float32
                )
                result = put(result, both, s)
        return result

    return on_device


def solution(mesh):
    n_fsdp, n_ctx = mesh.devices.shape
    n_core = 2
    n_y = len({d.coords[1] for d in mesh.devices.flat})
    n_z = n_fsdp // (n_core * n_y)
    split = Mesh(mesh.devices.reshape(n_y, n_z, n_core, n_ctx), ("y", "z", "core", "ctx"))
    rows = ("y", "z", "core", "ctx")
    placed = (
        P(rows, None),
        P(rows, None),
        P(rows, None),
        P(),
        P(("y", "z", "core"), "ctx"),
    )
    return jax.shard_map(
        make_on_device(n_ctx, n_core),
        mesh=split,
        in_specs=placed,
        out_specs=P(("y", "z", "core"), "ctx"),
        check_vma=False,
    )
```
